256 devices in a mesh: ctx: 64 (over y, z_lo, x), tp: 4 (over z_hi, core).
Axes of the slice: x: 4, y: 4, z: 8 (z_hi: 2, z_lo: 4; z = z_hi * 4 + z_lo), core: 2. Of those that a mesh axis runs over, the one named last changes fastest.
Arguments:
- activations: bfloat16 [40960, 4096], P('ctx', 'tp'), may hold values from -6 to 6
- group_counts: int32 [64], replicated, may hold values from 1 to 5, as said below
- genome_starts: int32 [32], replicated, may hold values from 0 to 24448, as said below
- in_weight: bfloat16 [4096, 3, 2048], P('ctx', None, 'tp'), may hold values from -0.09375 to 0.09375
- short_taps: float32 [7, 3, 2048], P(None, None, 'tp'), may hold values from -2 to 2
- long_taps: float32 [128, 2048], P(None, 'tp'), may hold values from -0.5 to 0.5
- out_weight: bfloat16 [2048, 4096], P('tp', 'ctx'), may hold values from -0.125 to 0.125
Outputs:
- block_out: bfloat16 [40960, 4096], P('ctx', 'tp')
The draws below stay inside these ranges and needn't reach their ends.
Inputs may be any that keep to these rules, and one draw needn't show every extreme that they name: Every device holds 1 or more blocks; group_counts[2k] + group_counts[2k+1] = 6 for every k. `genome_starts`: strictly increasing; the first entry is 0 and the last is exactly 24448.
All inputs are finite; a program needn't handle non-finite values.
Results may differ from the reference program's by a relative error of at most 0.012.
Values may be sent and summed in bfloat16 or wider, within the bound.
No kernel may reach another device: no remote copies, remote signals or barrier semaphores. Data moves between devices by JAX's collectives and lax.ppermute only.
A program may use at most 128 MiB of HBM per device.

```python
import jax
import jax.numpy as jnp
from jax import lax

D = 4096
C = 2048
GROUP = 128
MEAN = 3
SLOTS = 5
ROWS = 40960
TOTAL = 24576
GENOMES = 32
N_CTX = 64


def draw_group_counts(key, part):
    pairs = N_CTX // 2
    lower = jax.random.randint(jax.random.fold_in(key, 11), (pairs,), 1, 2 * MEAN)
    chosen = jax.random.randint(jax.random.fold_in(key, 12), (), 0, pairs)
    flipped = jax.random.randint(jax.random.fold_in(key, 13), (), 0, 2)
    extreme = jnp.where(flipped == 0, 2 * MEAN - 1, 1)
    lower = jnp.where(jnp.arange(pairs) == chosen, extreme, lower)
    return jnp.stack([lower, 2 * MEAN - lower], axis=1).reshape(N_CTX).astype(jnp.int32)


def draw_genome_starts(key, part):
    last_start = TOTAL - GROUP
    picked = jax.random.permutation(jax.random.fold_in(key, 21), last_start - 1)[:GENOMES - 2] + 1
    return jnp.concatenate([jnp.zeros((1,), jnp.int32), jnp.sort(picked).astype(jnp.int32), jnp.full((1,), last_start, jnp.int32)])


def levels(own_key, extent, shards, smallest, top_value):
    def one(position, blocks):
        steps = jax.random.uniform(jax.random.fold_in(jax.random.fold_in(own_key, 6), position), (blocks,), jnp.float32, smallest / len(shards), top_value / len(shards))
        return jnp.repeat(jnp.exp(steps), extent[position] // blocks).reshape((-1,) + (1,) * (len(extent) - position - 1))

    factor_of = one(*shards[0])
    for cut in shards[1:]:
        factor_of = factor_of * one(*cut)
    return factor_of


def scatter_about(key, extent, scale, limit, shards=(), held_as=jnp.bfloat16):
    level = levels(key, extent, shards, -0.22, 0.18) if shards else 1.0
    entries = jax.random.normal(key, extent, jnp.float32) * scale * level
    return jnp.minimum(jnp.maximum(entries, -limit), limit).astype(held_as)


def setup_inputs(seed: int = 0) -> dict:
    streams_of = jax.random.split(jax.random.key(seed), 8)
    return {
        "activations": scatter_about(streams_of[0], (ROWS, D), 1.0, 6.0, ((0, 64), (1, 4))),
        "group_counts": draw_group_counts(jax.random.fold_in(streams_of[7], 71), 0),
        "genome_starts": draw_genome_starts(jax.random.fold_in(streams_of[7], 71), 0),
        "in_weight": scatter_about(streams_of[3], (D, 3, C), D ** -0.5, 0.09375, ((0, 64), (2, 4))),
        "short_taps": scatter_about(streams_of[4], (7, 3, C), 0.38, 2.0, ((2, 4),), jnp.float32),
        "long_taps": scatter_about(streams_of[5], (128, C), 0.088, 0.5, ((1, 4),), jnp.float32),
        "out_weight": scatter_about(streams_of[6], (C, D), C ** -0.5, 0.125, ((0, 4), (1, 64))),
    }


def causal_taps(padded, taps, positions, gstart, width):
    count = positions.shape[0]
    shape = (count,) + (1,) * (padded.ndim - 1)
    summed = jnp.zeros(padded.shape[:0] + (count,) + padded.shape[1:], jnp.float32)
    for j in range(width):
        in_genome = (positions - j >= gstart).reshape(shape)
        window = padded[width - 1 - j:width - 1 - j + count]
        summed = summed + jnp.where(in_genome, window * taps[j], jnp.float32(0.0))
    return summed

def reference(activations, group_counts, genome_starts, in_weight, short_taps, long_taps, out_weight):
    ends = jnp.cumsum(group_counts).astype(jnp.int32)
    offsets = (ends - group_counts).astype(jnp.int32)
    packed = jnp.arange(TOTAL, dtype=jnp.int32)
    group_ids = packed // GROUP
    owners = lax.optimization_barrier(jnp.sum((ends[None, :] <= group_ids[:, None]).astype(jnp.int32), axis=1)).astype(jnp.int32)
    slot_rows = (owners * (SLOTS * GROUP) + (group_ids - offsets[owners]) * GROUP + packed % GROUP).astype(jnp.int32)
    seq_rows = activations[slot_rows]
    found = (jnp.searchsorted(genome_starts, packed, side='right') - 1).astype(jnp.int32)
    gstart = genome_starts[found]
    widened = seq_rows.astype(jnp.float32)
    normed = (widened * lax.rsqrt(lax.optimization_barrier(jnp.mean(widened * widened, axis=1, keepdims=True)) + 1e-06)).astype(jnp.bfloat16)
    width_d = in_weight.shape[0]
    branches = in_weight.shape[1]
    chans = in_weight.shape[2]
    projected = jnp.dot(normed, in_weight.reshape(width_d, branches * chans), preferred_element_type=jnp.float32)
    projected = projected.astype(jnp.bfloat16).reshape(TOTAL, branches, chans)
    padded = jnp.concatenate([jnp.zeros((6, branches, chans), jnp.float32), projected.astype(jnp.float32)], axis=0)
    feat = causal_taps(padded, short_taps, packed, gstart, 7)
    mixed = (feat[:, 1] * feat[:, 2]).astype(jnp.bfloat16)
    padded_long = jnp.concatenate([jnp.zeros((127, chans), jnp.float32), mixed.astype(jnp.float32)], axis=0)
    filtered = causal_taps(padded_long, long_taps, packed, gstart, 128)
    gated = (feat[:, 0] * filtered).astype(jnp.bfloat16)
    branch_out = jnp.dot(gated, out_weight, preferred_element_type=jnp.float32)
    seq_out = (widened + branch_out).astype(jnp.bfloat16)
    return jnp.zeros(activations.shape, jnp.bfloat16).at[slot_rows].set(seq_out)
```

```python
import jax
import jax.numpy as jnp
from jax import lax
from jax.sharding import PartitionSpec as P

GROUP = 128


def passed_along(shard, axis, by):
    peers = lax.axis_size(axis)
    pairs = [(i, i + by) for i in range(peers) if 0 <= i + by < peers]
    return lax.ppermute(shard, axis, pairs)


def genome_start(positions, genome_starts):
    above = genome_starts[None, :] <= positions[:, None]
    return jnp.max(jnp.where(above, genome_starts[None, :], 0), axis=1)


def causal_taps(padded, taps, positions, gstart, width):
    count = positions.shape[0]
    shape = (count,) + (1,) * (padded.ndim - 1)
    summed = jnp.zeros((count,) + padded.shape[1:], jnp.float32)
    for j in range(width):
        in_genome = (positions - j >= gstart).reshape(shape)
        window = padded[width - 1 - j : width - 1 - j + count]
        summed = summed + jnp.where(in_genome, window * taps[j], jnp.float32(0.0))
    return summed


def body(activations, group_counts, genome_starts, in_weight, short_taps, long_taps, out_weight):
    ctx_size = lax.axis_size("ctx")
    my_index = lax.axis_index("ctx")
    own_rows = activations.shape[0]
    device_ids = jnp.arange(ctx_size, dtype=jnp.int32)
    own_count = jnp.sum(jnp.where(device_ids == my_index, group_counts, 0))
    offset = jnp.sum(jnp.where(device_ids < my_index, group_counts, 0))
    row_ids = jnp.arange(own_rows, dtype=jnp.int32)
    positions = offset * GROUP + row_ids
    tail_end = own_count * GROUP

    def last_rows(source, count):
        return lax.dynamic_slice_in_dim(source, tail_end - count, count, 0)

    gstart = genome_start(positions, genome_starts)
    all_feats = lax.all_gather(activations, "tp", axis=1, tiled=True)
    widened = all_feats.astype(jnp.float32)
    normed = (
        widened * lax.rsqrt(jnp.mean(widened * widened, axis=1, keepdims=True) + 1e-06)
    ).astype(jnp.bfloat16)
    row_count = normed.shape[0]
    branches = in_weight.shape[1]
    chans = in_weight.shape[2]
    local_in = in_weight.reshape(in_weight.shape[0], branches * chans)
    both = jnp.concatenate([local_in, out_weight.T], axis=1)
    both_rows = lax.all_gather(both, "ctx", axis=0, tiled=True)
    flat = both_rows[:, : branches * chans]
    out_rows = both_rows[:, branches * chans :]
    summed = jnp.dot(normed, flat, preferred_element_type=jnp.float32)
    projected = summed.astype(jnp.bfloat16).reshape(row_count, branches, chans)
    rim_short = passed_along(last_rows(projected, 6), "ctx", 1)
    feat = causal_taps(
        jnp.concatenate([rim_short, projected], axis=0).astype(jnp.float32),
        short_taps,
        positions,
        gstart,
        7,
    )
    mixed = (feat[:, 1] * feat[:, 2]).astype(jnp.bfloat16)
    rim_long = passed_along(last_rows(mixed, 127), "ctx", 1)
    filtered = causal_taps(
        jnp.concatenate([rim_long, mixed], axis=0).astype(jnp.float32),
        long_taps,
        positions,
        gstart,
        128,
    )
    gated = (feat[:, 0] * filtered).astype(jnp.bfloat16)
    partial_out = lax.dot_general(
        gated,
        out_rows,
        (((1,), (1,)), ((), ())),
        preferred_element_type=jnp.float32,
    )
    branch_out = lax.psum_scatter(
        partial_out.astype(jnp.bfloat16), "tp", scatter_dimension=1, tiled=True
    ).astype(jnp.float32)
    result = (activations.astype(jnp.float32) + branch_out).astype(jnp.bfloat16)
    slot_ids = jnp.arange(own_rows, dtype=jnp.int32)
    live_rows = (slot_ids < own_count * GROUP)[:, None]
    return jnp.where(live_rows, result, jnp.zeros_like(result))


def solution(mesh):
    placed = (
        P("ctx", "tp"),
        P(),
        P(),
        P("ctx", None, "tp"),
        P(None, None, "tp"),
        P(None, "tp"),
        P("tp", "ctx"),
    )
    return jax.shard_map(
        body, mesh=mesh, in_specs=placed, out_specs=P("ctx", "tp"), check_vma=False
    )
```

```python
import jax
import jax.numpy as jnp
from jax import lax
from jax.sharding import PartitionSpec as P

GROUP = 128
CTX = ("y", "zl", "x")
TP = ("zh", "core")


def passed_along(shard, axis, by):
    peers = lax.axis_size(axis)
    pairs = [(i, i + by) for i in range(peers) if 0 <= i + by < peers]
    return lax.ppermute(shard, axis, pairs)


def genome_start(positions, genome_starts):
    above = genome_starts[None, :] <= positions[:, None]
    return jnp.max(jnp.where(above, genome_starts[None, :], 0), axis=1)


def causal_taps(padded, taps, positions, gstart, width):
    count = positions.shape[0]
    shape = (count,) + (1,) * (padded.ndim - 1)
    summed = jnp.zeros((count,) + padded.shape[1:], jnp.float32)
    for j in range(width):
        in_genome = (positions - j >= gstart).reshape(shape)
        window = padded[width - 1 - j : width - 1 - j + count]
        summed = summed + jnp.where(in_genome, window * taps[j], jnp.float32(0.0))
    return summed


def body(activations, group_counts, genome_starts, in_weight, short_taps, long_taps, out_weight):
    ctx_size = lax.axis_size(CTX)
    my_index = lax.axis_index(CTX)
    own_rows = activations.shape[0]
    device_ids = jnp.arange(ctx_size, dtype=jnp.int32)
    own_count = jnp.sum(jnp.where(device_ids == my_index, group_counts, 0))
    offset = jnp.sum(jnp.where(device_ids < my_index, group_counts, 0))
    row_ids = jnp.arange(own_rows, dtype=jnp.int32)
    positions = offset * GROUP + row_ids
    tail_end = own_count * GROUP

    def last_rows(source, count):
        return lax.dynamic_slice_in_dim(source, tail_end - count, count, 0)

    gstart = genome_start(positions, genome_starts)
    all_feats = lax.all_gather(activations, TP, axis=1, tiled=True)
    widened = all_feats.astype(jnp.float32)
    normed = (
        widened * lax.rsqrt(jnp.mean(widened * widened, axis=1, keepdims=True) + 1e-06)
    ).astype(jnp.bfloat16)
    row_count = normed.shape[0]
    branches = in_weight.shape[1]
    chans = in_weight.shape[2]
    local_in = in_weight.reshape(in_weight.shape[0], branches * chans)
    both = jnp.concatenate([local_in, out_weight.T], axis=1)
    both_rows = both
    for part in reversed(CTX):
        both_rows = lax.all_gather(both_rows, part, axis=0, tiled=True)
    flat = both_rows[:, : branches * chans]
    out_rows = both_rows[:, branches * chans :]
    summed = jnp.dot(normed, flat, preferred_element_type=jnp.float32)
    projected = summed.astype(jnp.bfloat16).reshape(row_count, branches, chans)
    rim_short = passed_along(last_rows(projected, 6), CTX, 1)
    feat = causal_taps(
        jnp.concatenate([rim_short, projected], axis=0).astype(jnp.float32),
        short_taps,
        positions,
        gstart,
        7,
    )
    mixed = (feat[:, 1] * feat[:, 2]).astype(jnp.bfloat16)
    rim_long = passed_along(last_rows(mixed, 127), CTX, 1)
    filtered = causal_taps(
        jnp.concatenate([rim_long, mixed], axis=0).astype(jnp.float32),
        long_taps,
        positions,
        gstart,
        128,
    )
    gated = (feat[:, 0] * filtered).astype(jnp.bfloat16)
    partial_out = lax.dot_general(
        gated,
        out_rows,
        (((1,), (1,)), ((), ())),
        preferred_element_type=jnp.float32,
    )
    branch_out = lax.psum_scatter(
        partial_out.astype(jnp.bfloat16), TP, scatter_dimension=1, tiled=True
    ).astype(jnp.float32)
    result = (activations.astype(jnp.float32) + branch_out).astype(jnp.bfloat16)
    slot_ids = jnp.arange(own_rows, dtype=jnp.int32)
    live_rows = (slot_ids < own_count * GROUP)[:, None]
    return jnp.where(live_rows, result, jnp.zeros_like(result))


def solution(mesh):
    fine = jax.sharding.Mesh(mesh.devices.reshape(4, 4, 4, 2, 2), CTX + TP)
    placed = (
        P(CTX, TP),
        P(),
        P(),
        P(CTX, None, TP),
        P(None, None, TP),
        P(None, TP),
        P(TP, CTX),
    )
    return jax.shard_map(
        body, mesh=fine, in_specs=placed, out_specs=P(CTX, TP), check_vma=False
    )
```

```python
import jax
import jax.numpy as jnp
from jax import lax
from jax.sharding import PartitionSpec as P

GROUP = 128
PAIR_BLOCKS = 6
CTX = ("y", "zl", "x")
TP = ("zh", "core")


def passed_along(shard, axis, by):
    peers = lax.axis_size(axis)
    pairs = [(i, i + by) for i in range(peers) if 0 <= i + by < peers]
    return lax.ppermute(shard, axis, pairs)


def swapped(shard, axis):
    peers = lax.axis_size(axis)
    pairs = [(i, i ^ 1) for i in range(peers)]
    return lax.ppermute(shard, axis, pairs)


def shifted(source, offset, count):
    width = source.shape[1:]
    pad = 2 * count
    zeros = jnp.zeros((pad,) + width, source.dtype)
    padded = jnp.concatenate([zeros, source, zeros], axis=0)
    start = jnp.clip(pad + offset, 0, padded.shape[0] - count)
    return lax.dynamic_slice_in_dim(padded, start, count, 0)


def spliced(first, first_off, first_len, second, second_off, count):
    rows = jnp.arange(count, dtype=jnp.int32).reshape((count,) + (1,) * (first.ndim - 1))
    return jnp.where(
        rows < first_len,
        shifted(first, first_off, count),
        shifted(second, second_off, count),
    )


def genome_start(positions, genome_starts):
    above = genome_starts[None, :] <= positions[:, None]
    return jnp.max(jnp.where(above, genome_starts[None, :], 0), axis=1)


def causal_taps(padded, taps, positions, gstart, width):
    count = positions.shape[0]
    shape = (count,) + (1,) * (padded.ndim - 1)
    summed = jnp.zeros((count,) + padded.shape[1:], jnp.float32)
    for j in range(width):
        in_genome = (positions - j >= gstart).reshape(shape)
        window = padded[width - 1 - j : width - 1 - j + count]
        summed = summed + jnp.where(in_genome, window * taps[j], jnp.float32(0.0))
    return summed


def body(activations, group_counts, genome_starts, in_weight, short_taps, long_taps, out_weight):
    my_index = lax.axis_index(CTX)
    own_rows = activations.shape[0]
    share = PAIR_BLOCKS * GROUP // 2
    window = own_rows - share
    parity = my_index % 2
    even_count = jnp.sum(
        jnp.where(jnp.arange(group_counts.shape[0]) == my_index - parity, group_counts, 0)
    )
    even_rows = even_count * GROUP
    own_count = jnp.where(parity == 0, even_count, PAIR_BLOCKS - even_count)

    sent = lax.dynamic_slice_in_dim(activations, (1 - parity) * share, window, 0)
    got = swapped(sent, CTX)
    x_even = spliced(activations, 0, even_rows, got, -even_rows, share)
    x_odd = spliced(got, 0, even_rows - share, activations, share - even_rows, share)
    x_own = jnp.where(parity == 0, x_even, x_odd)

    positions = my_index * share + jnp.arange(share, dtype=jnp.int32)

    def last_rows(source, count):
        return source[share - count :]

    gstart = genome_start(positions, genome_starts)
    all_feats = lax.all_gather(x_own, TP, axis=1, tiled=True)
    widened = all_feats.astype(jnp.float32)
    normed = (
        widened * lax.rsqrt(jnp.mean(widened * widened, axis=1, keepdims=True) + 1e-06)
    ).astype(jnp.bfloat16)
    row_count = normed.shape[0]
    branches = in_weight.shape[1]
    chans = in_weight.shape[2]
    local_in = in_weight.reshape(in_weight.shape[0], branches * chans)
    both = jnp.concatenate([local_in, out_weight.T], axis=1)
    both_rows = both
    for part in reversed(CTX):
        both_rows = lax.all_gather(both_rows, part, axis=0, tiled=True)
    flat = both_rows[:, : branches * chans]
    out_rows = both_rows[:, branches * chans :]
    summed = jnp.dot(normed, flat, preferred_element_type=jnp.float32)
    projected = summed.astype(jnp.bfloat16).reshape(row_count, branches, chans)
    rim_short = passed_along(last_rows(projected, 6), CTX, 1)
    feat = causal_taps(
        jnp.concatenate([rim_short, projected], axis=0).astype(jnp.float32),
        short_taps,
        positions,
        gstart,
        7,
    )
    mixed = (feat[:, 1] * feat[:, 2]).astype(jnp.bfloat16)
    rim_long = passed_along(last_rows(mixed, 127), CTX, 1)
    filtered = causal_taps(
        jnp.concatenate([rim_long, mixed], axis=0).astype(jnp.float32),
        long_taps,
        positions,
        gstart,
        128,
    )
    gated = (feat[:, 0] * filtered).astype(jnp.bfloat16)
    partial_out = lax.dot_general(
        gated,
        out_rows,
        (((1,), (1,)), ((), ())),
        preferred_element_type=jnp.float32,
    )
    branch_out = lax.psum_scatter(
        partial_out.astype(jnp.bfloat16), TP, scatter_dimension=1, tiled=True
    ).astype(jnp.float32)
    result = (x_own.astype(jnp.float32) + branch_out).astype(jnp.bfloat16)

    back = lax.dynamic_slice_in_dim(result, (1 - parity) * (share - window), window, 0)
    got_back = swapped(back, CTX)
    out_even = spliced(result, 0, share, got_back, -share, own_rows)
    out_odd = spliced(
        got_back,
        even_rows - (share - window),
        share - even_rows,
        result,
        even_rows - share,
        own_rows,
    )
    placed_rows = jnp.where(parity == 0, out_even, out_odd)
    slot_ids = jnp.arange(own_rows, dtype=jnp.int32)
    live_rows = (slot_ids < own_count * GROUP)[:, None]
    return jnp.where(live_rows, placed_rows, jnp.zeros_like(placed_rows))


def solution(mesh):
    fine = jax.sharding.Mesh(mesh.devices.reshape(4, 4, 4, 2, 2), CTX + TP)
    placed = (
        P(CTX, TP),
        P(),
        P(),
        P(CTX, None, TP),
        P(None, None, TP),
        P(None, TP),
        P(TP, CTX),
    )
    return jax.shard_map(
        body, mesh=fine, in_specs=placed, out_specs=P(CTX, TP), check_vma=False
    )
```

```python
import jax
import jax.numpy as jnp
from jax import lax
from jax.sharding import PartitionSpec as P

GROUP = 128
PAIR_BLOCKS = 6
CTX = ("y", "zl", "x")
TP = ("zh", "core")


def passed_along(shard, axis, by):
    peers = lax.axis_size(axis)
    pairs = [(i, i + by) for i in range(peers) if 0 <= i + by < peers]
    return lax.ppermute(shard, axis, pairs)


def swapped(shard, axis):
    peers = lax.axis_size(axis)
    pairs = [(i, i ^ 1) for i in range(peers)]
    return lax.ppermute(shard, axis, pairs)


def shifted(source, offset, count):
    width = source.shape[1:]
    pad = 2 * count
    zeros = jnp.zeros((pad,) + width, source.dtype)
    padded = jnp.concatenate([zeros, source, zeros], axis=0)
    start = jnp.clip(pad + offset, 0, padded.shape[0] - count)
    return lax.dynamic_slice_in_dim(padded, start, count, 0)


def spliced(first, first_off, first_len, second, second_off, count):
    rows = jnp.arange(count, dtype=jnp.int32).reshape((count,) + (1,) * (first.ndim - 1))
    return jnp.where(
        rows < first_len,
        shifted(first, first_off, count),
        shifted(second, second_off, count),
    )


def tp_blocks_gather(block, axis):
    peers = lax.axis_size(axis)
    me = lax.axis_index(axis)
    got = [block]
    for by in range(1, peers):
        got.append(lax.ppermute(block, axis, [(i, (i + by) % peers) for i in range(peers)]))
    stacked = jnp.stack(got)
    order = (me - jnp.arange(peers, dtype=jnp.int32)) % peers
    ordered = jnp.take(stacked, order, axis=0)
    return jnp.moveaxis(ordered, 0, 1).reshape(block.shape[0], peers * block.shape[1])


def tp_blocks_sum(full, axis):
    peers = lax.axis_size(axis)
    me = lax.axis_index(axis)
    width = full.shape[1] // peers
    blocks = full.reshape(full.shape[0], peers, width)
    total = lax.dynamic_index_in_dim(blocks, me, 1, keepdims=False).astype(jnp.float32)
    for by in range(1, peers):
        sent = lax.dynamic_index_in_dim(blocks, (me + by) % peers, 1, keepdims=False)
        got = lax.ppermute(sent, axis, [(i, (i + by) % peers) for i in range(peers)])
        total = total + got.astype(jnp.float32)
    return total


def genome_start(positions, genome_starts):
    above = genome_starts[None, :] <= positions[:, None]
    return jnp.max(jnp.where(above, genome_starts[None, :], 0), axis=1)


def causal_taps(padded, taps, positions, gstart, width):
    count = positions.shape[0]
    shape = (count,) + (1,) * (padded.ndim - 1)
    summed = jnp.zeros((count,) + padded.shape[1:], jnp.float32)
    for j in range(width):
        in_genome = (positions - j >= gstart).reshape(shape)
        window = padded[width - 1 - j : width - 1 - j + count]
        summed = summed + jnp.where(in_genome, window * taps[j], jnp.float32(0.0))
    return summed


def body(activations, group_counts, genome_starts, in_weight, short_taps, long_taps, out_weight):
    my_index = lax.axis_index(CTX)
    own_rows = activations.shape[0]
    share = PAIR_BLOCKS * GROUP // 2
    window = own_rows - share
    parity = my_index % 2
    even_count = jnp.sum(
        jnp.where(jnp.arange(group_counts.shape[0]) == my_index - parity, group_counts, 0)
    )
    even_rows = even_count * GROUP
    own_count = jnp.where(parity == 0, even_count, PAIR_BLOCKS - even_count)

    sent = lax.dynamic_slice_in_dim(activations, (1 - parity) * share, window, 0)
    got = swapped(sent, CTX)
    x_even = spliced(activations, 0, even_rows, got, -even_rows, share)
    x_odd = spliced(got, 0, even_rows - share, activations, share - even_rows, share)
    x_own = jnp.where(parity == 0, x_even, x_odd)

    positions = my_index * share + jnp.arange(share, dtype=jnp.int32)

    def last_rows(source, count):
        return source[share - count :]

    gstart = genome_start(positions, genome_starts)
    all_feats = tp_blocks_gather(x_own, TP)
    widened = all_feats.astype(jnp.float32)
    normed = (
        widened * lax.rsqrt(jnp.mean(widened * widened, axis=1, keepdims=True) + 1e-06)
    ).astype(jnp.bfloat16)
    row_count = normed.shape[0]
    branches = in_weight.shape[1]
    chans = in_weight.shape[2]
    local_in = in_weight.reshape(in_weight.shape[0], branches * chans)
    both = jnp.concatenate([local_in, out_weight.T], axis=1)
    both_rows = both
    for part in reversed(CTX):
        both_rows = lax.all_gather(both_rows, part, axis=0, tiled=True)
    flat = both_rows[:, : branches * chans]
    out_rows = both_rows[:, branches * chans :]
    summed = jnp.dot(normed, flat, preferred_element_type=jnp.float32)
    projected = summed.astype(jnp.bfloat16).reshape(row_count, branches, chans)
    rim_short = passed_along(last_rows(projected, 6), CTX, 1)
    feat = causal_taps(
        jnp.concatenate([rim_short, projected], axis=0).astype(jnp.float32),
        short_taps,
        positions,
        gstart,
        7,
    )
    mixed = (feat[:, 1] * feat[:, 2]).astype(jnp.bfloat16)
    rim_long = passed_along(last_rows(mixed, 127), CTX, 1)
    filtered = causal_taps(
        jnp.concatenate([rim_long, mixed], axis=0).astype(jnp.float32),
        long_taps,
        positions,
        gstart,
        128,
    )
    gated = (feat[:, 0] * filtered).astype(jnp.bfloat16)
    partial_out = lax.dot_general(
        gated,
        out_rows,
        (((1,), (1,)), ((), ())),
        preferred_element_type=jnp.float32,
    )
    branch_out = tp_blocks_sum(partial_out.astype(jnp.bfloat16), TP)
    result = (x_own.astype(jnp.float32) + branch_out).astype(jnp.bfloat16)

    back = lax.dynamic_slice_in_dim(result, (1 - parity) * (share - window), window, 0)
    got_back = swapped(back, CTX)
    out_even = spliced(result, 0, share, got_back, -share, own_rows)
    out_odd = spliced(
        got_back,
        even_rows - (share - window),
        share - even_rows,
        result,
        even_rows - share,
        own_rows,
    )
    placed_rows = jnp.where(parity == 0, out_even, out_odd)
    slot_ids = jnp.arange(own_rows, dtype=jnp.int32)
    live_rows = (slot_ids < own_count * GROUP)[:, None]
    return jnp.where(live_rows, placed_rows, jnp.zeros_like(placed_rows))


def solution(mesh):
    fine = jax.sharding.Mesh(mesh.devices.reshape(4, 4, 4, 2, 2), CTX + TP)
    placed = (
        P(CTX, TP),
        P(),
        P(),
        P(CTX, None, TP),
        P(None, None, TP),
        P(None, TP),
        P(TP, CTX),
    )
    return jax.shard_map(
        body, mesh=fine, in_specs=placed, out_specs=P(CTX, TP), check_vma=False
    )
```

```python
import jax
import jax.numpy as jnp
from jax import lax
from jax.sharding import PartitionSpec as P

GROUP = 128
PAIR_BLOCKS = 6
CTX = ("y", "zl", "x")
TP = ("zh", "core")
GATHER_ORDER = ("zl", "x", "y")


def passed_along(shard, axis, by):
    peers = lax.axis_size(axis)
    pairs = [(i, i + by) for i in range(peers) if 0 <= i + by < peers]
    return lax.ppermute(shard, axis, pairs)


def swapped(shard, axis):
    peers = lax.axis_size(axis)
    pairs = [(i, i ^ 1) for i in range(peers)]
    return lax.ppermute(shard, axis, pairs)


def shifted(source, offset, count):
    width = source.shape[1:]
    pad = 2 * count
    zeros = jnp.zeros((pad,) + width, source.dtype)
    padded = jnp.concatenate([zeros, source, zeros], axis=0)
    start = jnp.clip(pad + offset, 0, padded.shape[0] - count)
    return lax.dynamic_slice_in_dim(padded, start, count, 0)


def spliced(first, first_off, first_len, second, second_off, count):
    rows = jnp.arange(count, dtype=jnp.int32).reshape((count,) + (1,) * (first.ndim - 1))
    return jnp.where(
        rows < first_len,
        shifted(first, first_off, count),
        shifted(second, second_off, count),
    )


def tp_blocks_gather(block, axis):
    peers = lax.axis_size(axis)
    me = lax.axis_index(axis)
    got = [block]
    for by in range(1, peers):
        got.append(lax.ppermute(block, axis, [(i, (i + by) % peers) for i in range(peers)]))
    stacked = jnp.stack(got)
    order = (me - jnp.arange(peers, dtype=jnp.int32)) % peers
    ordered = jnp.take(stacked, order, axis=0)
    return jnp.moveaxis(ordered, 0, 1).reshape(block.shape[0], peers * block.shape[1])


def tp_blocks_sum(full, axis):
    peers = lax.axis_size(axis)
    me = lax.axis_index(axis)
    width = full.shape[1] // peers
    blocks = full.reshape(full.shape[0], peers, width)
    total = lax.dynamic_index_in_dim(blocks, me, 1, keepdims=False).astype(jnp.float32)
    for by in range(1, peers):
        sent = lax.dynamic_index_in_dim(blocks, (me + by) % peers, 1, keepdims=False)
        got = lax.ppermute(sent, axis, [(i, (i + by) % peers) for i in range(peers)])
        total = total + got.astype(jnp.float32)
    return total


def genome_start(positions, genome_starts):
    above = genome_starts[None, :] <= positions[:, None]
    return jnp.max(jnp.where(above, genome_starts[None, :], 0), axis=1)


def causal_taps(padded, taps, positions, gstart, width):
    count = positions.shape[0]
    shape = (count,) + (1,) * (padded.ndim - 1)
    summed = jnp.zeros((count,) + padded.shape[1:], jnp.float32)
    for j in range(width):
        in_genome = (positions - j >= gstart).reshape(shape)
        window = padded[width - 1 - j : width - 1 - j + count]
        summed = summed + jnp.where(in_genome, window * taps[j], jnp.float32(0.0))
    return summed


def body(activations, group_counts, genome_starts, in_weight, short_taps, long_taps, out_weight):
    my_index = lax.axis_index(CTX)
    own_rows = activations.shape[0]
    share = PAIR_BLOCKS * GROUP // 2
    window = own_rows - share
    parity = my_index % 2
    even_count = jnp.sum(
        jnp.where(jnp.arange(group_counts.shape[0]) == my_index - parity, group_counts, 0)
    )
    even_rows = even_count * GROUP
    own_count = jnp.where(parity == 0, even_count, PAIR_BLOCKS - even_count)

    sent = lax.dynamic_slice_in_dim(activations, (1 - parity) * share, window, 0)
    got = swapped(sent, CTX)
    x_even = spliced(activations, 0, even_rows, got, -even_rows, share)
    x_odd = spliced(got, 0, even_rows - share, activations, share - even_rows, share)
    x_own = jnp.where(parity == 0, x_even, x_odd)

    positions = my_index * share + jnp.arange(share, dtype=jnp.int32)

    def last_rows(source, count):
        return source[share - count :]

    gstart = genome_start(positions, genome_starts)
    all_feats = tp_blocks_gather(x_own, TP)
    widened = all_feats.astype(jnp.float32)
    normed = (
        widened * lax.rsqrt(jnp.mean(widened * widened, axis=1, keepdims=True) + 1e-06)
    ).astype(jnp.bfloat16)
    row_count = normed.shape[0]
    branches = in_weight.shape[1]
    chans = in_weight.shape[2]
    local_in = in_weight.reshape(in_weight.shape[0], branches * chans)
    both = jnp.concatenate([local_in, out_weight.T], axis=1)
    both_rows = both
    for part in GATHER_ORDER:
        both_rows = lax.all_gather(both_rows, part, axis=0, tiled=True)
    ny, nz, nx = (lax.axis_size(a) for a in CTX)
    block = in_weight.shape[0]
    flat = both_rows[:, : branches * chans]
    normed = (
        normed.reshape(row_count, ny, nz, nx, block)
        .transpose(0, 1, 3, 2, 4)
        .reshape(row_count, ny * nz * nx * block)
    )
    out_rows = (
        both_rows[:, branches * chans :]
        .reshape(ny, nx, nz, block, -1)
        .transpose(0, 2, 1, 3, 4)
        .reshape(ny * nz * nx * block, -1)
    )
    summed = jnp.dot(normed, flat, preferred_element_type=jnp.float32)
    projected = summed.astype(jnp.bfloat16).reshape(row_count, branches, chans)
    rim_short = passed_along(last_rows(projected, 6), CTX, 1)
    feat = causal_taps(
        jnp.concatenate([rim_short, projected], axis=0).astype(jnp.float32),
        short_taps,
        positions,
        gstart,
        7,
    )
    mixed = (feat[:, 1] * feat[:, 2]).astype(jnp.bfloat16)
    rim_long = passed_along(last_rows(mixed, 127), CTX, 1)
    filtered = causal_taps(
        jnp.concatenate([rim_long, mixed], axis=0).astype(jnp.float32),
        long_taps,
        positions,
        gstart,
        128,
    )
    gated = (feat[:, 0] * filtered).astype(jnp.bfloat16)
    partial_out = lax.dot_general(
        gated,
        out_rows,
        (((1,), (1,)), ((), ())),
        preferred_element_type=jnp.float32,
    )
    branch_out = tp_blocks_sum(partial_out.astype(jnp.bfloat16), TP)
    result = (x_own.astype(jnp.float32) + branch_out).astype(jnp.bfloat16)

    back = lax.dynamic_slice_in_dim(result, (1 - parity) * (share - window), window, 0)
    got_back = swapped(back, CTX)
    out_even = spliced(result, 0, share, got_back, -share, own_rows)
    out_odd = spliced(
        got_back,
        even_rows - (share - window),
        share - even_rows,
        result,
        even_rows - share,
        own_rows,
    )
    placed_rows = jnp.where(parity == 0, out_even, out_odd)
    slot_ids = jnp.arange(own_rows, dtype=jnp.int32)
    live_rows = (slot_ids < own_count * GROUP)[:, None]
    return jnp.where(live_rows, placed_rows, jnp.zeros_like(placed_rows))


def solution(mesh):
    fine = jax.sharding.Mesh(mesh.devices.reshape(4, 4, 4, 2, 2), CTX + TP)
    placed = (
        P(CTX, TP),
        P(),
        P(),
        P(CTX, None, TP),
        P(None, None, TP),
        P(None, TP),
        P(TP, CTX),
    )
    return jax.shard_map(
        body, mesh=fine, in_specs=placed, out_specs=P(CTX, TP), check_vma=False
    )
```

```python
import jax
import jax.numpy as jnp
from jax import lax
from jax.sharding import PartitionSpec as P

GROUP = 128
PAIR_BLOCKS = 6
CTX = ("y", "zl", "x")
TP = ("zh", "core")
GATHER_ORDER = ("zl", "x", "y")


def passed_along(shard, axis, by):
    peers = lax.axis_size(axis)
    pairs = [(i, i + by) for i in range(peers) if 0 <= i + by < peers]
    return lax.ppermute(shard, axis, pairs)


def swapped(shard, axis):
    peers = lax.axis_size(axis)
    pairs = [(i, i ^ 1) for i in range(peers)]
    return lax.ppermute(shard, axis, pairs)


def from_row(source, start, count):
    width = source.shape[1:]
    padded = jnp.concatenate([source, jnp.zeros((count,) + width, source.dtype)], axis=0)
    return lax.dynamic_slice_in_dim(padded, jnp.clip(start, 0, source.shape[0]), count, 0)


def tp_blocks_gather(block, axis):
    peers = lax.axis_size(axis)
    me = lax.axis_index(axis)
    got = [block]
    for by in range(1, peers):
        got.append(lax.ppermute(block, axis, [(i, (i + by) % peers) for i in range(peers)]))
    stacked = jnp.stack(got)
    order = (me - jnp.arange(peers, dtype=jnp.int32)) % peers
    ordered = jnp.take(stacked, order, axis=0)
    return jnp.moveaxis(ordered, 0, 1).reshape(block.shape[0], peers * block.shape[1])


def tp_blocks_sum(full, axis):
    peers = lax.axis_size(axis)
    me = lax.axis_index(axis)
    width = full.shape[1] // peers
    blocks = full.reshape(full.shape[0], peers, width)
    total = lax.dynamic_index_in_dim(blocks, me, 1, keepdims=False).astype(jnp.float32)
    for by in range(1, peers):
        sent = lax.dynamic_index_in_dim(blocks, (me + by) % peers, 1, keepdims=False)
        got = lax.ppermute(sent, axis, [(i, (i + by) % peers) for i in range(peers)])
        total = total + got.astype(jnp.float32)
    return total


def genome_start(positions, genome_starts):
    above = genome_starts[None, :] <= positions[:, None]
    return jnp.max(jnp.where(above, genome_starts[None, :], 0), axis=1)


def causal_taps(padded, taps, positions, gstart, width):
    count = positions.shape[0]
    shape = (count,) + (1,) * (padded.ndim - 1)
    summed = jnp.zeros((count,) + padded.shape[1:], jnp.float32)
    for j in range(width):
        in_genome = (positions - j >= gstart).reshape(shape)
        window = padded[width - 1 - j : width - 1 - j + count]
        summed = summed + jnp.where(in_genome, window * taps[j], jnp.float32(0.0))
    return summed


def body(activations, group_counts, genome_starts, in_weight, short_taps, long_taps, out_weight):
    my_index = lax.axis_index(CTX)
    own_rows = activations.shape[0]
    share = PAIR_BLOCKS * GROUP // 2
    window = own_rows - share
    parity = my_index % 2
    even_count = jnp.sum(
        jnp.where(jnp.arange(group_counts.shape[0]) == my_index - parity, group_counts, 0)
    )
    even_rows = even_count * GROUP
    own_count = jnp.where(parity == 0, even_count, PAIR_BLOCKS - even_count)

    sent = lax.dynamic_slice_in_dim(activations, (1 - parity) * share, window, 0)
    got = swapped(sent, CTX)
    rows = jnp.arange(share, dtype=jnp.int32)[:, None]
    zeros_front = jnp.zeros((share,) + activations.shape[1:], activations.dtype)
    x_even = jnp.where(
        rows < even_rows,
        activations[:share],
        from_row(jnp.concatenate([zeros_front, got], axis=0), share - even_rows, share),
    )
    x_odd = jnp.where(
        rows < even_rows - share,
        from_row(got, 0, share),
        from_row(
            jnp.concatenate([zeros_front[:window], activations], axis=0),
            own_rows - even_rows,
            share,
        ),
    )
    x_own = jnp.where(parity == 0, x_even, x_odd)

    positions = my_index * share + jnp.arange(share, dtype=jnp.int32)

    def last_rows(source, count):
        return source[share - count :]

    gstart = genome_start(positions, genome_starts)
    all_feats = tp_blocks_gather(x_own, TP)
    widened = all_feats.astype(jnp.float32)
    normed = (
        widened * lax.rsqrt(jnp.mean(widened * widened, axis=1, keepdims=True) + 1e-06)
    ).astype(jnp.bfloat16)
    row_count = normed.shape[0]
    branches = in_weight.shape[1]
    chans = in_weight.shape[2]
    local_in = in_weight.reshape(in_weight.shape[0], branches * chans)
    both = jnp.concatenate([local_in, out_weight.T], axis=1)
    both_rows = both
    for part in GATHER_ORDER:
        both_rows = lax.all_gather(both_rows, part, axis=0, tiled=True)
    ny, nz, nx = (lax.axis_size(a) for a in CTX)
    block = in_weight.shape[0]
    flat = both_rows[:, : branches * chans]
    normed = (
        normed.reshape(row_count, ny, nz, nx, block)
        .transpose(0, 1, 3, 2, 4)
        .reshape(row_count, ny * nz * nx * block)
    )
    out_rows = (
        both_rows[:, branches * chans :]
        .reshape(ny, nx, nz, block, -1)
        .transpose(0, 2, 1, 3, 4)
        .reshape(ny * nz * nx * block, -1)
    )
    summed = jnp.dot(normed, flat, preferred_element_type=jnp.float32)
    projected = summed.astype(jnp.bfloat16).reshape(row_count, branches, chans)
    rim_short = passed_along(last_rows(projected, 6), CTX, 1)
    feat = causal_taps(
        jnp.concatenate([rim_short, projected], axis=0).astype(jnp.float32),
        short_taps,
        positions,
        gstart,
        7,
    )
    mixed = (feat[:, 1] * feat[:, 2]).astype(jnp.bfloat16)
    rim_long = passed_along(last_rows(mixed, 127), CTX, 1)
    long_in = jnp.concatenate([rim_long, mixed], axis=0).astype(jnp.float32)
    half = share // 2
    results = []
    for h in range(2):
        lo = h * half
        filtered = causal_taps(
            long_in[lo : lo + half + 127],
            long_taps,
            positions[lo : lo + half],
            gstart[lo : lo + half],
            128,
        )
        gated = (feat[lo : lo + half, 0] * filtered).astype(jnp.bfloat16)
        partial_out = lax.dot_general(
            gated,
            out_rows,
            (((1,), (1,)), ((), ())),
            preferred_element_type=jnp.float32,
        )
        branch_out = tp_blocks_sum(partial_out.astype(jnp.bfloat16), TP)
        results.append(
            (x_own[lo : lo + half].astype(jnp.float32) + branch_out).astype(jnp.bfloat16)
        )
    result = jnp.concatenate(results, axis=0)

    back = lax.dynamic_slice_in_dim(result, (1 - parity) * (share - window), window, 0)
    got_back = swapped(back, CTX)
    out_even = jnp.concatenate([result, got_back], axis=0)
    out_odd = from_row(
        jnp.concatenate([got_back, result], axis=0), even_rows - (share - window), own_rows
    )
    placed_rows = jnp.where(parity == 0, out_even, out_odd)
    slot_ids = jnp.arange(own_rows, dtype=jnp.int32)
    live_rows = (slot_ids < own_count * GROUP)[:, None]
    return jnp.where(live_rows, placed_rows, jnp.zeros_like(placed_rows))


def solution(mesh):
    fine = jax.sharding.Mesh(mesh.devices.reshape(4, 4, 4, 2, 2), CTX + TP)
    placed = (
        P(CTX, TP),
        P(),
        P(),
        P(CTX, None, TP),
        P(None, None, TP),
        P(None, TP),
        P(TP, CTX),
    )
    return jax.shard_map(
        body, mesh=fine, in_specs=placed, out_specs=P(CTX, TP), check_vma=False
    )
```

```python
import jax
import jax.numpy as jnp
from jax import lax
from jax.sharding import PartitionSpec as P

GROUP = 128
PAIR_BLOCKS = 6
CTX = ("y", "zl", "x")
TP = ("zh", "core")
GATHER_ORDER = ("zl", "x", "y")


def passed_along(shard, axis, by):
    peers = lax.axis_size(axis)
    pairs = [(i, i + by) for i in range(peers) if 0 <= i + by < peers]
    return lax.ppermute(shard, axis, pairs)


def swapped(shard, axis):
    peers = lax.axis_size(axis)
    pairs = [(i, i ^ 1) for i in range(peers)]
    return lax.ppermute(shard, axis, pairs)


def from_row(source, start, count):
    width = source.shape[1:]
    padded = jnp.concatenate([source, jnp.zeros((count,) + width, source.dtype)], axis=0)
    return lax.dynamic_slice_in_dim(padded, jnp.clip(start, 0, source.shape[0]), count, 0)


def tp_blocks_gather(block, axis):
    peers = lax.axis_size(axis)
    me = lax.axis_index(axis)
    got = [block]
    for by in range(1, peers):
        got.append(lax.ppermute(block, axis, [(i, (i + by) % peers) for i in range(peers)]))
    stacked = jnp.stack(got)
    order = (me - jnp.arange(peers, dtype=jnp.int32)) % peers
    ordered = jnp.take(stacked, order, axis=0)
    return jnp.moveaxis(ordered, 0, 1).reshape(block.shape[0], peers * block.shape[1])


def tp_blocks_swap(blocks, axis):
    peers = lax.axis_size(axis)
    me = lax.axis_index(axis)
    got = [lax.dynamic_index_in_dim(blocks, me, 0, keepdims=False)]
    for by in range(1, peers):
        sent = lax.dynamic_index_in_dim(blocks, (me + by) % peers, 0, keepdims=False)
        got.append(lax.ppermute(sent, axis, [(i, (i + by) % peers) for i in range(peers)]))
    stacked = jnp.stack(got)
    order = (me - jnp.arange(peers, dtype=jnp.int32)) % peers
    ordered = jnp.take(stacked, order, axis=0)
    return jnp.moveaxis(ordered, 0, 1).reshape(blocks.shape[1], peers * blocks.shape[2])


def tp_blocks_sum(full, axis):
    peers = lax.axis_size(axis)
    me = lax.axis_index(axis)
    width = full.shape[1] // peers
    blocks = full.reshape(full.shape[0], peers, width)
    total = lax.dynamic_index_in_dim(blocks, me, 1, keepdims=False).astype(jnp.float32)
    for by in range(1, peers):
        sent = lax.dynamic_index_in_dim(blocks, (me + by) % peers, 1, keepdims=False)
        got = lax.ppermute(sent, axis, [(i, (i + by) % peers) for i in range(peers)])
        total = total + got.astype(jnp.float32)
    return total


def genome_start(positions, genome_starts):
    above = genome_starts[None, :] <= positions[:, None]
    return jnp.max(jnp.where(above, genome_starts[None, :], 0), axis=1)


def causal_taps(padded, taps, positions, gstart, width):
    count = positions.shape[0]
    shape = (count,) + (1,) * (padded.ndim - 1)
    summed = jnp.zeros((count,) + padded.shape[1:], jnp.float32)
    for j in range(width):
        in_genome = (positions - j >= gstart).reshape(shape)
        window = padded[width - 1 - j : width - 1 - j + count]
        summed = summed + jnp.where(in_genome, window * taps[j], jnp.float32(0.0))
    return summed


def body(activations, group_counts, genome_starts, in_weight, short_taps, long_taps, out_weight):
    my_index = lax.axis_index(CTX)
    own_rows = activations.shape[0]
    share = PAIR_BLOCKS * GROUP // 2
    window = own_rows - share
    parity = my_index % 2
    even_count = jnp.sum(
        jnp.where(jnp.arange(group_counts.shape[0]) == my_index - parity, group_counts, 0)
    )
    even_rows = even_count * GROUP
    own_count = jnp.where(parity == 0, even_count, PAIR_BLOCKS - even_count)

    sent = lax.dynamic_slice_in_dim(activations, (1 - parity) * share, window, 0)
    got = swapped(sent, CTX)
    rows = jnp.arange(share, dtype=jnp.int32)[:, None]
    zeros_front = jnp.zeros((share,) + activations.shape[1:], activations.dtype)
    x_even = jnp.where(
        rows < even_rows,
        activations[:share],
        from_row(jnp.concatenate([zeros_front, got], axis=0), share - even_rows, share),
    )
    x_odd = jnp.where(
        rows < even_rows - share,
        from_row(got, 0, share),
        from_row(
            jnp.concatenate([zeros_front[:window], activations], axis=0),
            own_rows - even_rows,
            share,
        ),
    )
    x_own = jnp.where(parity == 0, x_even, x_odd)

    positions = my_index * share + jnp.arange(share, dtype=jnp.int32)

    def last_rows(source, count):
        return source[share - count :]

    gstart = genome_start(positions, genome_starts)
    all_feats = tp_blocks_gather(x_own, TP)
    widened = all_feats.astype(jnp.float32)
    normed = (
        widened * lax.rsqrt(jnp.mean(widened * widened, axis=1, keepdims=True) + 1e-06)
    ).astype(jnp.bfloat16)
    row_count = normed.shape[0]
    branches = in_weight.shape[1]
    chans = in_weight.shape[2]
    local_in = in_weight.reshape(in_weight.shape[0], branches * chans)
    both = jnp.concatenate([local_in, out_weight.T], axis=1)
    both_rows = both
    for part in GATHER_ORDER:
        both_rows = lax.all_gather(both_rows, part, axis=0, tiled=True)
    ny, nz, nx = (lax.axis_size(a) for a in CTX)
    block = in_weight.shape[0]
    flat = both_rows[:, : branches * chans]
    normed = (
        normed.reshape(row_count, ny, nz, nx, block)
        .transpose(0, 1, 3, 2, 4)
        .reshape(row_count, ny * nz * nx * block)
    )
    out_rows = (
        both_rows[:, branches * chans :]
        .reshape(ny, nx, nz, block, -1)
        .transpose(0, 2, 1, 3, 4)
        .reshape(ny * nz * nx * block, -1)
    )
    summed = jnp.dot(normed, flat, preferred_element_type=jnp.float32)
    projected = summed.astype(jnp.bfloat16).reshape(row_count, branches, chans)
    rim_short = passed_along(last_rows(projected, 6), CTX, 1)
    feat = causal_taps(
        jnp.concatenate([rim_short, projected], axis=0).astype(jnp.float32),
        short_taps,
        positions,
        gstart,
        7,
    )
    mixed = (feat[:, 1] * feat[:, 2]).astype(jnp.bfloat16)
    rim_long = passed_along(last_rows(mixed, 127), CTX, 1)
    filtered = causal_taps(
        jnp.concatenate([rim_long, mixed], axis=0).astype(jnp.float32),
        long_taps,
        positions,
        gstart,
        128,
    )
    gated = (feat[:, 0] * filtered).astype(jnp.bfloat16)
    feats = x_own.shape[1]
    my_cols = tp_blocks_swap(out_rows.reshape(-1, feats, chans), TP)
    gated_all = tp_blocks_gather(gated, TP)
    branch_out = lax.dot_general(
        gated_all,
        my_cols,
        (((1,), (1,)), ((), ())),
        preferred_element_type=jnp.float32,
    )
    result = (x_own.astype(jnp.float32) + branch_out).astype(jnp.bfloat16)

    back = lax.dynamic_slice_in_dim(result, (1 - parity) * (share - window), window, 0)
    got_back = swapped(back, CTX)
    out_even = jnp.concatenate([result, got_back], axis=0)
    out_odd = from_row(
        jnp.concatenate([got_back, result], axis=0), even_rows - (share - window), own_rows
    )
    placed_rows = jnp.where(parity == 0, out_even, out_odd)
    slot_ids = jnp.arange(own_rows, dtype=jnp.int32)
    live_rows = (slot_ids < own_count * GROUP)[:, None]
    return jnp.where(live_rows, placed_rows, jnp.zeros_like(placed_rows))


def solution(mesh):
    fine = jax.sharding.Mesh(mesh.devices.reshape(4, 4, 4, 2, 2), CTX + TP)
    placed = (
        P(CTX, TP),
        P(),
        P(),
        P(CTX, None, TP),
        P(None, None, TP),
        P(None, TP),
        P(TP, CTX),
    )
    return jax.shard_map(
        body, mesh=fine, in_specs=placed, out_specs=P(CTX, TP), check_vma=False
    )
```

```python
import jax
import jax.numpy as jnp
from jax import lax
from jax.sharding import PartitionSpec as P

GROUP = 128
PAIR_BLOCKS = 6
CTX = ("y", "zl", "x")
TP = ("zh", "core")
GATHER_ORDER = ("zl", "x", "y")


def passed_along(shard, axis, by):
    peers = lax.axis_size(axis)
    pairs = [(i, i + by) for i in range(peers) if 0 <= i + by < peers]
    return lax.ppermute(shard, axis, pairs)


def swapped(shard, axis):
    peers = lax.axis_size(axis)
    pairs = [(i, i ^ 1) for i in range(peers)]
    return lax.ppermute(shard, axis, pairs)


def from_row(source, start, count):
    width = source.shape[1:]
    padded = jnp.concatenate([source, jnp.zeros((count,) + width, source.dtype)], axis=0)
    return lax.dynamic_slice_in_dim(padded, jnp.clip(start, 0, source.shape[0]), count, 0)


def ring_gather(block, axis):
    peers = lax.axis_size(axis)
    me = lax.axis_index(axis)
    got = [block]
    for by in range(1, peers):
        got.append(lax.ppermute(block, axis, [(i, (i + by) % peers) for i in range(peers)]))
    stacked = jnp.stack(got)
    order = (me - jnp.arange(peers, dtype=jnp.int32)) % peers
    return jnp.take(stacked, order, axis=0).reshape((peers * block.shape[0],) + block.shape[1:])


def tp_blocks_gather(block, axis):
    peers = lax.axis_size(axis)
    me = lax.axis_index(axis)
    got = [block]
    for by in range(1, peers):
        got.append(lax.ppermute(block, axis, [(i, (i + by) % peers) for i in range(peers)]))
    stacked = jnp.stack(got)
    order = (me - jnp.arange(peers, dtype=jnp.int32)) % peers
    ordered = jnp.take(stacked, order, axis=0)
    return jnp.moveaxis(ordered, 0, 1).reshape(block.shape[0], peers * block.shape[1])


def tp_blocks_sum(full, axis):
    peers = lax.axis_size(axis)
    me = lax.axis_index(axis)
    width = full.shape[1] // peers
    blocks = full.reshape(full.shape[0], peers, width)
    total = lax.dynamic_index_in_dim(blocks, me, 1, keepdims=False).astype(jnp.float32)
    for by in range(1, peers):
        sent = lax.dynamic_index_in_dim(blocks, (me + by) % peers, 1, keepdims=False)
        got = lax.ppermute(sent, axis, [(i, (i + by) % peers) for i in range(peers)])
        total = total + got.astype(jnp.float32)
    return total


def genome_start(positions, genome_starts):
    above = genome_starts[None, :] <= positions[:, None]
    return jnp.max(jnp.where(above, genome_starts[None, :], 0), axis=1)


def causal_taps(padded, taps, positions, gstart, width):
    count = positions.shape[0]
    shape = (count,) + (1,) * (padded.ndim - 1)
    summed = jnp.zeros((count,) + padded.shape[1:], jnp.float32)
    for j in range(width):
        in_genome = (positions - j >= gstart).reshape(shape)
        window = padded[width - 1 - j : width - 1 - j + count]
        summed = summed + jnp.where(in_genome, window * taps[j], jnp.float32(0.0))
    return summed


def body(activations, group_counts, genome_starts, in_weight, short_taps, long_taps, out_weight):
    my_index = lax.axis_index(CTX)
    own_rows = activations.shape[0]
    share = PAIR_BLOCKS * GROUP // 2
    window = own_rows - share
    parity = my_index % 2
    even_count = jnp.sum(
        jnp.where(jnp.arange(group_counts.shape[0]) == my_index - parity, group_counts, 0)
    )
    even_rows = even_count * GROUP
    own_count = jnp.where(parity == 0, even_count, PAIR_BLOCKS - even_count)

    sent = lax.dynamic_slice_in_dim(activations, (1 - parity) * share, window, 0)
    got = swapped(sent, CTX)
    rows = jnp.arange(share, dtype=jnp.int32)[:, None]
    zeros_front = jnp.zeros((share,) + activations.shape[1:], activations.dtype)
    x_even = jnp.where(
        rows < even_rows,
        activations[:share],
        from_row(jnp.concatenate([zeros_front, got], axis=0), share - even_rows, share),
    )
    x_odd = jnp.where(
        rows < even_rows - share,
        from_row(got, 0, share),
        from_row(
            jnp.concatenate([zeros_front[:window], activations], axis=0),
            own_rows - even_rows,
            share,
        ),
    )
    x_own = jnp.where(parity == 0, x_even, x_odd)

    positions = my_index * share + jnp.arange(share, dtype=jnp.int32)

    def last_rows(source, count):
        return source[share - count :]

    gstart = genome_start(positions, genome_starts)
    all_feats = tp_blocks_gather(x_own, TP)
    widened = all_feats.astype(jnp.float32)
    normed = (
        widened * lax.rsqrt(jnp.mean(widened * widened, axis=1, keepdims=True) + 1e-06)
    ).astype(jnp.bfloat16)
    row_count = normed.shape[0]
    branches = in_weight.shape[1]
    chans = in_weight.shape[2]
    local_in = in_weight.reshape(in_weight.shape[0], branches * chans)
    flat = local_in
    for part in GATHER_ORDER:
        flat = lax.all_gather(flat, part, axis=0, tiled=True)
    ny, nz, nx = (lax.axis_size(a) for a in CTX)
    block = in_weight.shape[0]
    normed = (
        normed.reshape(row_count, ny, nz, nx, block)
        .transpose(0, 1, 3, 2, 4)
        .reshape(row_count, ny * nz * nx * block)
    )
    out_rows = out_weight.T
    for part in ("y", "zl", "x"):
        out_rows = ring_gather(out_rows, part)
    out_rows = (
        out_rows.reshape(nx, nz, ny, block, -1)
        .transpose(2, 1, 0, 3, 4)
        .reshape(ny * nz * nx * block, -1)
    )
    summed = jnp.dot(normed, flat, preferred_element_type=jnp.float32)
    projected = summed.astype(jnp.bfloat16).reshape(row_count, branches, chans)
    rim_short = passed_along(last_rows(projected, 6), CTX, 1)
    feat = causal_taps(
        jnp.concatenate([rim_short, projected], axis=0).astype(jnp.float32),
        short_taps,
        positions,
        gstart,
        7,
    )
    mixed = (feat[:, 1] * feat[:, 2]).astype(jnp.bfloat16)
    rim_long = passed_along(last_rows(mixed, 127), CTX, 1)
    filtered = causal_taps(
        jnp.concatenate([rim_long, mixed], axis=0).astype(jnp.float32),
        long_taps,
        positions,
        gstart,
        128,
    )
    gated = (feat[:, 0] * filtered).astype(jnp.bfloat16)
    partial_out = lax.dot_general(
        gated,
        out_rows,
        (((1,), (1,)), ((), ())),
        preferred_element_type=jnp.float32,
    )
    branch_out = tp_blocks_sum(partial_out.astype(jnp.bfloat16), TP)
    result = (x_own.astype(jnp.float32) + branch_out).astype(jnp.bfloat16)

    back = lax.dynamic_slice_in_dim(result, (1 - parity) * (share - window), window, 0)
    got_back = swapped(back, CTX)
    out_even = jnp.concatenate([result, got_back], axis=0)
    out_odd = from_row(
        jnp.concatenate([got_back, result], axis=0), even_rows - (share - window), own_rows
    )
    placed_rows = jnp.where(parity == 0, out_even, out_odd)
    slot_ids = jnp.arange(own_rows, dtype=jnp.int32)
    live_rows = (slot_ids < own_count * GROUP)[:, None]
    return jnp.where(live_rows, placed_rows, jnp.zeros_like(placed_rows))


def solution(mesh):
    fine = jax.sharding.Mesh(mesh.devices.reshape(4, 4, 4, 2, 2), CTX + TP)
    placed = (
        P(CTX, TP),
        P(),
        P(),
        P(CTX, None, TP),
        P(None, None, TP),
        P(None, TP),
        P(TP, CTX),
    )
    return jax.shard_map(
        body, mesh=fine, in_specs=placed, out_specs=P(CTX, TP), check_vma=False
    )
```

```python
import jax
import jax.numpy as jnp
from jax import lax
from jax.sharding import PartitionSpec as P

GROUP = 128
PAIR_BLOCKS = 6
CTX = ("y", "zl", "x")
TP = ("zh", "core")
GATHER_ORDER = ("zl", "x", "y")


def passed_along(shard, axis, by):
    peers = lax.axis_size(axis)
    pairs = [(i, i + by) for i in range(peers) if 0 <= i + by < peers]
    return lax.ppermute(shard, axis, pairs)


def swapped(shard, axis):
    peers = lax.axis_size(axis)
    pairs = [(i, i ^ 1) for i in range(peers)]
    return lax.ppermute(shard, axis, pairs)


def from_row(source, start, count):
    width = source.shape[1:]
    padded = jnp.concatenate([source, jnp.zeros((count,) + width, source.dtype)], axis=0)
    return lax.dynamic_slice_in_dim(padded, jnp.clip(start, 0, source.shape[0]), count, 0)


def ring_gather(block, axis):
    peers = lax.axis_size(axis)
    me = lax.axis_index(axis)
    got = [block]
    for by in range(1, peers):
        got.append(lax.ppermute(block, axis, [(i, (i + by) % peers) for i in range(peers)]))
    stacked = jnp.stack(got)
    order = (me - jnp.arange(peers, dtype=jnp.int32)) % peers
    return jnp.take(stacked, order, axis=0).reshape((peers * block.shape[0],) + block.shape[1:])


def tp_blocks_gather(block, axis):
    peers = lax.axis_size(axis)
    me = lax.axis_index(axis)
    got = [block]
    for by in range(1, peers):
        got.append(lax.ppermute(block, axis, [(i, (i + by) % peers) for i in range(peers)]))
    stacked = jnp.stack(got)
    order = (me - jnp.arange(peers, dtype=jnp.int32)) % peers
    ordered = jnp.take(stacked, order, axis=0)
    return jnp.moveaxis(ordered, 0, 1).reshape(block.shape[0], peers * block.shape[1])


def tp_projected_sum(gated, out_rows, axis):
    peers = lax.axis_size(axis)
    me = lax.axis_index(axis)
    width = out_rows.shape[0] // peers

    def block_for(k):
        rows = lax.dynamic_slice_in_dim(out_rows, k * width, width, 0)
        part = lax.dot_general(
            gated, rows, (((1,), (1,)), ((), ())), preferred_element_type=jnp.float32
        )
        return part.astype(jnp.bfloat16)

    total = block_for(me).astype(jnp.float32)
    for by in range(1, peers):
        sent = block_for((me + by) % peers)
        got = lax.ppermute(sent, axis, [(i, (i + by) % peers) for i in range(peers)])
        total = total + got.astype(jnp.float32)
    return total


def genome_start(positions, genome_starts):
    above = genome_starts[None, :] <= positions[:, None]
    return jnp.max(jnp.where(above, genome_starts[None, :], 0), axis=1)


def causal_taps(padded, taps, positions, gstart, width):
    count = positions.shape[0]
    shape = (count,) + (1,) * (padded.ndim - 1)
    summed = jnp.zeros((count,) + padded.shape[1:], jnp.float32)
    for j in range(width):
        in_genome = (positions - j >= gstart).reshape(shape)
        window = padded[width - 1 - j : width - 1 - j + count]
        summed = summed + jnp.where(in_genome, window * taps[j], jnp.float32(0.0))
    return summed


def body(activations, group_counts, genome_starts, in_weight, short_taps, long_taps, out_weight):
    my_index = lax.axis_index(CTX)
    own_rows = activations.shape[0]
    share = PAIR_BLOCKS * GROUP // 2
    window = own_rows - share
    parity = my_index % 2
    even_count = jnp.sum(
        jnp.where(jnp.arange(group_counts.shape[0]) == my_index - parity, group_counts, 0)
    )
    even_rows = even_count * GROUP
    own_count = jnp.where(parity == 0, even_count, PAIR_BLOCKS - even_count)

    sent = lax.dynamic_slice_in_dim(activations, (1 - parity) * share, window, 0)
    got = swapped(sent, CTX)
    rows = jnp.arange(share, dtype=jnp.int32)[:, None]
    zeros_front = jnp.zeros((share,) + activations.shape[1:], activations.dtype)
    x_even = jnp.where(
        rows < even_rows,
        activations[:share],
        from_row(jnp.concatenate([zeros_front, got], axis=0), share - even_rows, share),
    )
    x_odd = jnp.where(
        rows < even_rows - share,
        from_row(got, 0, share),
        from_row(
            jnp.concatenate([zeros_front[:window], activations], axis=0),
            own_rows - even_rows,
            share,
        ),
    )
    x_own = jnp.where(parity == 0, x_even, x_odd)

    positions = my_index * share + jnp.arange(share, dtype=jnp.int32)

    def last_rows(source, count):
        return source[share - count :]

    gstart = genome_start(positions, genome_starts)
    all_feats = tp_blocks_gather(x_own, TP)
    widened = all_feats.astype(jnp.float32)
    normed = (
        widened * lax.rsqrt(jnp.mean(widened * widened, axis=1, keepdims=True) + 1e-06)
    ).astype(jnp.bfloat16)
    row_count = normed.shape[0]
    branches = in_weight.shape[1]
    chans = in_weight.shape[2]
    local_in = in_weight.reshape(in_weight.shape[0], branches * chans)
    flat = local_in
    for part in GATHER_ORDER:
        flat = lax.all_gather(flat, part, axis=0, tiled=True)
    ny, nz, nx = (lax.axis_size(a) for a in CTX)
    block = in_weight.shape[0]
    normed = (
        normed.reshape(row_count, ny, nz, nx, block)
        .transpose(0, 1, 3, 2, 4)
        .reshape(row_count, ny * nz * nx * block)
    )
    out_rows = out_weight.T
    for part in ("y", "zl", "x"):
        out_rows = ring_gather(out_rows, part)
    out_rows = (
        out_rows.reshape(nx, nz, ny, block, -1)
        .transpose(2, 1, 0, 3, 4)
        .reshape(ny * nz * nx * block, -1)
    )
    summed = jnp.dot(normed, flat, preferred_element_type=jnp.float32)
    projected = summed.astype(jnp.bfloat16).reshape(row_count, branches, chans)
    rim_short = passed_along(last_rows(projected, 6), CTX, 1)
    feat = causal_taps(
        jnp.concatenate([rim_short, projected], axis=0).astype(jnp.float32),
        short_taps,
        positions,
        gstart,
        7,
    )
    mixed = (feat[:, 1] * feat[:, 2]).astype(jnp.bfloat16)
    rim_long = passed_along(last_rows(mixed, 127), CTX, 1)
    filtered = causal_taps(
        jnp.concatenate([rim_long, mixed], axis=0).astype(jnp.float32),
        long_taps,
        positions,
        gstart,
        128,
    )
    gated = (feat[:, 0] * filtered).astype(jnp.bfloat16)
    branch_out = tp_projected_sum(gated, out_rows, TP)
    result = (x_own.astype(jnp.float32) + branch_out).astype(jnp.bfloat16)

    back = lax.dynamic_slice_in_dim(result, (1 - parity) * (share - window), window, 0)
    got_back = swapped(back, CTX)
    out_even = jnp.concatenate([result, got_back], axis=0)
    out_odd = from_row(
        jnp.concatenate([got_back, result], axis=0), even_rows - (share - window), own_rows
    )
    placed_rows = jnp.where(parity == 0, out_even, out_odd)
    slot_ids = jnp.arange(own_rows, dtype=jnp.int32)
    live_rows = (slot_ids < own_count * GROUP)[:, None]
    return jnp.where(live_rows, placed_rows, jnp.zeros_like(placed_rows))


def solution(mesh):
    fine = jax.sharding.Mesh(mesh.devices.reshape(4, 4, 4, 2, 2), CTX + TP)
    placed = (
        P(CTX, TP),
        P(),
        P(),
        P(CTX, None, TP),
        P(None, None, TP),
        P(None, TP),
        P(TP, CTX),
    )
    return jax.shard_map(
        body, mesh=fine, in_specs=placed, out_specs=P(CTX, TP), check_vma=False
    )
```

```python
import jax
import jax.numpy as jnp
from jax import lax
from jax.sharding import PartitionSpec as P

GROUP = 128
PAIR_BLOCKS = 6
CTX = ("y", "zl", "x")
TP = ("zh", "core")
GATHER_ORDER = ("zl", "x", "y")


def passed_along(shard, axis, by):
    peers = lax.axis_size(axis)
    pairs = [(i, i + by) for i in range(peers) if 0 <= i + by < peers]
    return lax.ppermute(shard, axis, pairs)


def swapped(shard, axis):
    peers = lax.axis_size(axis)
    pairs = [(i, i ^ 1) for i in range(peers)]
    return lax.ppermute(shard, axis, pairs)


def from_row(source, start, count):
    width = source.shape[1:]
    padded = jnp.concatenate([source, jnp.zeros((count,) + width, source.dtype)], axis=0)
    return lax.dynamic_slice_in_dim(padded, jnp.clip(start, 0, source.shape[0]), count, 0)


def ring_gather(block, axis):
    peers = lax.axis_size(axis)
    me = lax.axis_index(axis)
    got = [block]
    for by in range(1, peers):
        got.append(lax.ppermute(block, axis, [(i, (i + by) % peers) for i in range(peers)]))
    stacked = jnp.stack(got)
    order = (me - jnp.arange(peers, dtype=jnp.int32)) % peers
    return jnp.take(stacked, order, axis=0).reshape((peers * block.shape[0],) + block.shape[1:])


def partner(block, axis):
    return lax.ppermute(block, axis, [(0, 1), (1, 0)])


def ordered_pair(mine, theirs, me):
    return jnp.where(me == 0, jnp.stack([mine, theirs]), jnp.stack([theirs, mine]))


def tp_blocks_gather(block, axis):
    hi, lo = axis
    zh = lax.axis_index(hi)
    core = lax.axis_index(lo)
    by_zh = ordered_pair(block, partner(block, hi), zh)
    by_core = ordered_pair(by_zh, partner(by_zh, lo), core)
    ordered = jnp.swapaxes(by_core, 0, 1).reshape((4,) + block.shape)
    return jnp.moveaxis(ordered, 0, 1).reshape(block.shape[0], 4 * block.shape[1])


def tp_projected_sum(gated, out_rows, axis):
    hi, lo = axis
    zh = lax.axis_index(hi)
    core = lax.axis_index(lo)
    width = out_rows.shape[0] // 4

    def block_for(k):
        rows = lax.dynamic_slice_in_dim(out_rows, k * width, width, 0)
        part = lax.dot_general(
            gated, rows, (((1,), (1,)), ((), ())), preferred_element_type=jnp.float32
        )
        return part.astype(jnp.bfloat16)

    mine = jnp.stack([block_for(core), block_for(2 + core)])
    theirs = jnp.stack([block_for(1 - core), block_for(3 - core)])
    pair_sum = mine.astype(jnp.float32) + partner(theirs, lo).astype(jnp.float32)
    keep = lax.dynamic_index_in_dim(pair_sum, zh, 0, keepdims=False)
    send = lax.dynamic_index_in_dim(pair_sum, 1 - zh, 0, keepdims=False)
    return keep + partner(send.astype(jnp.bfloat16), hi).astype(jnp.float32)


def genome_start(positions, genome_starts):
    above = genome_starts[None, :] <= positions[:, None]
    return jnp.max(jnp.where(above, genome_starts[None, :], 0), axis=1)


def causal_taps(padded, taps, positions, gstart, width):
    count = positions.shape[0]
    shape = (count,) + (1,) * (padded.ndim - 1)
    summed = jnp.zeros((count,) + padded.shape[1:], jnp.float32)
    for j in range(width):
        in_genome = (positions - j >= gstart).reshape(shape)
        window = padded[width - 1 - j : width - 1 - j + count]
        summed = summed + jnp.where(in_genome, window * taps[j], jnp.float32(0.0))
    return summed


def body(activations, group_counts, genome_starts, in_weight, short_taps, long_taps, out_weight):
    my_index = lax.axis_index(CTX)
    own_rows = activations.shape[0]
    share = PAIR_BLOCKS * GROUP // 2
    window = own_rows - share
    parity = my_index % 2
    even_count = jnp.sum(
        jnp.where(jnp.arange(group_counts.shape[0]) == my_index - parity, group_counts, 0)
    )
    even_rows = even_count * GROUP
    own_count = jnp.where(parity == 0, even_count, PAIR_BLOCKS - even_count)

    sent = lax.dynamic_slice_in_dim(activations, (1 - parity) * share, window, 0)
    got = swapped(sent, CTX)
    rows = jnp.arange(share, dtype=jnp.int32)[:, None]
    zeros_front = jnp.zeros((share,) + activations.shape[1:], activations.dtype)
    x_even = jnp.where(
        rows < even_rows,
        activations[:share],
        from_row(jnp.concatenate([zeros_front, got], axis=0), share - even_rows, share),
    )
    x_odd = jnp.where(
        rows < even_rows - share,
        from_row(got, 0, share),
        from_row(
            jnp.concatenate([zeros_front[:window], activations], axis=0),
            own_rows - even_rows,
            share,
        ),
    )
    x_own = jnp.where(parity == 0, x_even, x_odd)

    positions = my_index * share + jnp.arange(share, dtype=jnp.int32)

    def last_rows(source, count):
        return source[share - count :]

    gstart = genome_start(positions, genome_starts)
    all_feats = tp_blocks_gather(x_own, TP)
    widened = all_feats.astype(jnp.float32)
    normed = (
        widened * lax.rsqrt(jnp.mean(widened * widened, axis=1, keepdims=True) + 1e-06)
    ).astype(jnp.bfloat16)
    row_count = normed.shape[0]
    branches = in_weight.shape[1]
    chans = in_weight.shape[2]
    local_in = in_weight.reshape(in_weight.shape[0], branches * chans)
    flat = local_in
    for part in GATHER_ORDER:
        flat = lax.all_gather(flat, part, axis=0, tiled=True)
    ny, nz, nx = (lax.axis_size(a) for a in CTX)
    block = in_weight.shape[0]
    normed = (
        normed.reshape(row_count, ny, nz, nx, block)
        .transpose(0, 1, 3, 2, 4)
        .reshape(row_count, ny * nz * nx * block)
    )
    out_rows = out_weight.T
    for part in ("y", "zl", "x"):
        out_rows = ring_gather(out_rows, part)
    out_rows = (
        out_rows.reshape(nx, nz, ny, block, -1)
        .transpose(2, 1, 0, 3, 4)
        .reshape(ny * nz * nx * block, -1)
    )
    summed = jnp.dot(normed, flat, preferred_element_type=jnp.float32)
    projected = summed.astype(jnp.bfloat16).reshape(row_count, branches, chans)
    rim_short = passed_along(last_rows(projected, 6), CTX, 1)
    feat = causal_taps(
        jnp.concatenate([rim_short, projected], axis=0).astype(jnp.float32),
        short_taps,
        positions,
        gstart,
        7,
    )
    mixed = (feat[:, 1] * feat[:, 2]).astype(jnp.bfloat16)
    rim_long = passed_along(last_rows(mixed, 127), CTX, 1)
    filtered = causal_taps(
        jnp.concatenate([rim_long, mixed], axis=0).astype(jnp.float32),
        long_taps,
        positions,
        gstart,
        128,
    )
    gated = (feat[:, 0] * filtered).astype(jnp.bfloat16)
    branch_out = tp_projected_sum(gated, out_rows, TP)
    result = (x_own.astype(jnp.float32) + branch_out).astype(jnp.bfloat16)

    back = lax.dynamic_slice_in_dim(result, (1 - parity) * (share - window), window, 0)
    got_back = swapped(back, CTX)
    out_even = jnp.concatenate([result, got_back], axis=0)
    out_odd = from_row(
        jnp.concatenate([got_back, result], axis=0), even_rows - (share - window), own_rows
    )
    placed_rows = jnp.where(parity == 0, out_even, out_odd)
    slot_ids = jnp.arange(own_rows, dtype=jnp.int32)
    live_rows = (slot_ids < own_count * GROUP)[:, None]
    return jnp.where(live_rows, placed_rows, jnp.zeros_like(placed_rows))


def solution(mesh):
    fine = jax.sharding.Mesh(mesh.devices.reshape(4, 4, 4, 2, 2), CTX + TP)
    placed = (
        P(CTX, TP),
        P(),
        P(),
        P(CTX, None, TP),
        P(None, None, TP),
        P(None, TP),
        P(TP, CTX),
    )
    return jax.shard_map(
        body, mesh=fine, in_specs=placed, out_specs=P(CTX, TP), check_vma=False
    )
```
